256 devices in a mesh: wide: 32 (over x, y, z_lo), narrow: 8 (over z_hi, core).
Axes of the slice: x: 4, y: 4, z: 8 (z_hi: 4, z_lo: 2; z = z_hi * 2 + z_lo), core: 2. Of those that a mesh axis runs over, the one named last changes fastest.
Arguments:
- r_matrix: bfloat16 [10240, 102400], P('narrow', 'wide'), may hold values from -0.01953125 to 0.01953125
- cmm_panel: bfloat16 [102400, 1280], P('wide', 'narrow'), may hold values from -18 to 18
- ctm_panel: bfloat16 [10240, 1280], P('narrow', 'wide'), may hold values from -18 to 18
- cee_in: float32 [10240, 10240], P('wide', 'narrow'), may hold values from -2 to 2
Outputs:
- cee_out: float32 [10240, 10240], P('wide', 'narrow')
The draws below stay inside these ranges and needn't reach their ends.
All inputs are finite; a program needn't handle non-finite values.
Results may differ from the reference program's by a relative error of at most 0.0022.
Values may be sent and summed in bfloat16 or wider, within the bound.
No kernel may reach another device: no remote copies, remote signals or barrier semaphores. Data moves between devices by JAX's collectives and lax.ppermute only.
A program may use at most 128 MiB of HBM per device.

```python
import jax
import jax.numpy as jnp
from jax import lax

NT = 10240
NM = 102400
KPW = 40
KP = 1280
MPD = 3200
N_WIDE = 32


def strengthened(entries, stream_key, source, target, blocks, factor):
    owner, partner = [(jnp.arange(entries.shape[axis_at]) // (entries.shape[axis_at] // blocks)).reshape([-1 if axis == axis_at else 1 for axis in range(entries.ndim)]) for axis_at in (source, target)]
    chosen = jax.random.permutation(stream_key, blocks)[partner]
    strong = (owner == chosen) | (owner == (partner + blocks // 2) % blocks)
    return jnp.where(strong, factor * entries, entries)


def block_levels(own_key, dims, cuts, smallest, high):
    loudness = 1.0
    for dim, blocks in cuts:
        draws = jax.random.uniform(jax.random.fold_in(jax.random.fold_in(own_key, 6), dim), (blocks,), jnp.float32, smallest / len(cuts), high / len(cuts))
        loudness = loudness * jnp.repeat(jnp.exp(draws), dims[dim] // blocks).reshape((-1,) + (1,) * (len(dims) - 1 - dim))
    return loudness


def noise(key, extent, scale, most, split=(), kind=jnp.bfloat16):
    values = jax.random.normal(key, extent, jnp.float32) * scale
    if len(split) > 0:
        values = block_levels(key, extent, split, -0.22, 0.18) * values
    return jnp.clip(values, min=-most, max=most).astype(kind)


def heavy_noise(rng, shape, width, reach, cuts, heavy, kind=jnp.bfloat16):
    result = width * jax.random.normal(rng, shape, jnp.float32)
    if cuts:
        result = result * block_levels(rng, shape, cuts, -0.22, 0.18)
    return jnp.clip(strengthened(result, jax.random.fold_in(rng, 3), *heavy), -reach, reach).astype(kind)


def setup_inputs(seed: int = 0) -> dict:
    key_list = jax.random.split(jax.random.key(seed), 5)
    r_matrix = noise(key_list[0], (NT, NM), NM ** -0.5, 0.01953125, ((0, 8), (1, 32)))
    cmm_panel = heavy_noise(key_list[1], (NM, KP), 3.0, 18.0, ((0, 32), (1, 8)), (0, 1, 32, 2.75))
    ctm_panel = noise(key_list[2], (NT, KP), 3.0, 18.0, ((0, 8), (1, 32)))
    cee_in = noise(key_list[3], (NT, NT), 0.3, 2.0, ((0, 32), (1, 8)), jnp.float32)
    return dict(r_matrix=r_matrix, cmm_panel=cmm_panel, ctm_panel=ctm_panel, cee_in=cee_in)


def reference(r_matrix, cmm_panel, ctm_panel, cee_in):
    r_three = r_matrix.reshape(NT, N_WIDE, MPD)
    r_panel = r_three[:, :, :KPW].reshape(NT, KP)

    def add_block(total, block):
        start = (block * MPD).astype(jnp.int32)
        rows = lax.dynamic_slice_in_dim(r_matrix, start, MPD, 1)
        cols = lax.dynamic_slice_in_dim(cmm_panel, start, MPD, 0)
        term = jnp.dot(rows, cols, preferred_element_type=jnp.float32)
        return total + term, None

    z_panel, unused = lax.scan(add_block, jnp.zeros((NT, KP), jnp.float32), jnp.arange(N_WIDE, dtype=jnp.int32))
    a_panel = (z_panel - ctm_panel.astype(jnp.float32)).astype(jnp.bfloat16)
    left = jnp.concatenate([a_panel, r_panel], axis=1)
    right = jnp.concatenate([r_panel, -ctm_panel], axis=1)
    update = lax.dot_general(left, right, (((1,), (1,)), ((), ())), preferred_element_type=jnp.float32)
    return cee_in + update
```

```python
import jax
import jax.numpy as jnp
from jax import lax
from jax.sharding import PartitionSpec as P


def per_device(r_matrix, cmm_panel, ctm_panel, cee_in, n_wide, n_narrow):
    slope_rows = r_matrix.shape[0]
    tile_rows = cee_in.shape[0]
    panel_width = ctm_panel.shape[1]
    piece = slope_rows // n_wide
    wide_index = lax.axis_index("wide")
    narrow_index = lax.axis_index("narrow")

    rc = jnp.concatenate([r_matrix[:, :panel_width], ctm_panel], axis=1)
    rc_all = lax.all_to_all(
        jnp.broadcast_to(rc[None], (n_wide,) + rc.shape), "wide", 0, 0, tiled=True
    )

    cmm_full = lax.all_gather(cmm_panel, "narrow", axis=1, tiled=True)
    z_part = jnp.dot(r_matrix, cmm_full, preferred_element_type=jnp.float32)

    z_recv = lax.all_to_all(
        z_part.reshape(n_wide, piece, z_part.shape[1]), "wide", 0, 0, tiled=True
    )
    z_mine = jnp.sum(z_recv, axis=0).reshape(piece, n_wide, panel_width)
    rc_rows = lax.dynamic_slice_in_dim(rc_all, wide_index * piece, piece, 1)
    rc_rows = jnp.transpose(rc_rows, (1, 0, 2))
    a_piece = (z_mine - rc_rows[:, :, panel_width:].astype(jnp.float32)).astype(jnp.bfloat16)
    left_piece = jnp.concatenate([a_piece, -rc_rows[:, :, :panel_width]], axis=2)

    blocks = n_wide // n_narrow
    perm = []
    for w in range(n_wide):
        for n in range(n_narrow):
            perm.append((w * n_narrow + n, (n * blocks + w // n_narrow) * n_narrow + w % n_narrow))
    left_piece = lax.ppermute(left_piece, ("wide", "narrow"), perm)
    left_rows = lax.all_gather(left_piece, "narrow", axis=0, tiled=True)

    update = lax.dot_general(
        left_rows, rc_all, (((1, 2), (0, 2)), ((), ())), preferred_element_type=jnp.float32
    )
    return cee_in + update


def solution(mesh):
    n_wide, n_narrow = mesh.shape["wide"], mesh.shape["narrow"]
    placed = (P("narrow", "wide"), P("wide", "narrow"), P("narrow", "wide"), P("wide", "narrow"))

    def body(r_matrix, cmm_panel, ctm_panel, cee_in):
        return per_device(r_matrix, cmm_panel, ctm_panel, cee_in, n_wide, n_narrow)

    return jax.shard_map(
        body, mesh=mesh, in_specs=placed, out_specs=P("wide", "narrow"), check_vma=False
    )
```

```python
import jax
import jax.numpy as jnp
from jax import lax
from jax.sharding import PartitionSpec as P


def per_device(r_matrix, cmm_panel, ctm_panel, cee_in, n_wide, n_narrow):
    slope_rows = r_matrix.shape[0]
    tile_rows = cee_in.shape[0]
    panel_width = ctm_panel.shape[1]
    piece = slope_rows // n_wide
    wide_index = lax.axis_index("wide")
    narrow_index = lax.axis_index("narrow")

    rc = jnp.concatenate([r_matrix[:, :panel_width], ctm_panel], axis=1)
    rc_all = lax.all_to_all(
        jnp.broadcast_to(rc[None], (n_wide,) + rc.shape), "wide", 0, 0, tiled=True
    )

    cmm_full = lax.all_gather(cmm_panel, "narrow", axis=1, tiled=True)
    z_part = jnp.dot(r_matrix, cmm_full, preferred_element_type=jnp.float32)

    z_recv = lax.all_to_all(
        z_part.reshape(n_wide, piece, z_part.shape[1]), "wide", 0, 0, tiled=True
    )
    z_mine = jnp.sum(z_recv, axis=0).reshape(piece, n_wide, panel_width)
    rc_rows = lax.dynamic_slice_in_dim(rc_all, wide_index * piece, piece, 1)
    rc_rows = jnp.transpose(rc_rows, (1, 0, 2))
    a_piece = (z_mine - rc_rows[:, :, panel_width:].astype(jnp.float32)).astype(jnp.bfloat16)
    left_piece = jnp.concatenate([a_piece, -rc_rows[:, :, :panel_width]], axis=2)

    blocks = n_wide // n_narrow
    perm = []
    for w in range(n_wide):
        for n in range(n_narrow):
            perm.append((w * n_narrow + n, (n * blocks + w // n_narrow) * n_narrow + w % n_narrow))
    arrived = []
    for shift in range(n_narrow):
        arrived.append(lax.ppermute(left_piece, ("wide", "narrow"), [
            (src, (dst // n_narrow) * n_narrow + (dst % n_narrow + shift) % n_narrow) for src, dst in perm
        ]))
    order = (narrow_index - jnp.arange(n_narrow)) % n_narrow
    left_rows = jnp.take(jnp.stack(arrived), order, axis=0).reshape((tile_rows,) + left_piece.shape[1:])

    update = lax.dot_general(
        left_rows, rc_all, (((1, 2), (0, 2)), ((), ())), preferred_element_type=jnp.float32
    )
    return cee_in + update


def solution(mesh):
    n_wide, n_narrow = mesh.shape["wide"], mesh.shape["narrow"]
    placed = (P("narrow", "wide"), P("wide", "narrow"), P("narrow", "wide"), P("wide", "narrow"))

    def body(r_matrix, cmm_panel, ctm_panel, cee_in):
        return per_device(r_matrix, cmm_panel, ctm_panel, cee_in, n_wide, n_narrow)

    return jax.shard_map(
        body, mesh=mesh, in_specs=placed, out_specs=P("wide", "narrow"), check_vma=False
    )
```

```python
import jax
import jax.numpy as jnp
from jax import lax
from jax.sharding import PartitionSpec as P

N_CHUNKS = 2


def per_device(r_matrix, cmm_panel, ctm_panel, cee_in, n_wide, n_narrow):
    slope_rows = r_matrix.shape[0]
    tile_rows = cee_in.shape[0]
    panel_width = ctm_panel.shape[1]
    cols = cmm_panel.shape[1]
    width = cols // N_CHUNKS
    piece = slope_rows // n_wide
    wide_index = lax.axis_index("wide")

    rc = jnp.concatenate([r_matrix[:, :panel_width], ctm_panel], axis=1)
    rc_all = lax.all_to_all(
        jnp.broadcast_to(rc[None], (n_wide,) + rc.shape), "wide", 0, 0, tiled=True
    )

    blocks = n_wide // n_narrow
    perm = []
    for w in range(n_wide):
        for n in range(n_narrow):
            perm.append((w * n_narrow + n, (n * blocks + w // n_narrow) * n_narrow + w % n_narrow))

    rc_rows = lax.all_to_all(rc.reshape(n_wide, piece, rc.shape[1]), "wide", 0, 0, tiled=True)
    rc_rows = jnp.transpose(rc_rows, (1, 0, 2))
    ctm_rows = rc_rows[:, :, panel_width:].astype(jnp.float32).reshape(
        piece, n_narrow, N_CHUNKS, width // panel_width, panel_width
    )
    r_rows = rc_rows[:, :, :panel_width].reshape(piece, n_wide * panel_width)

    zw = n_narrow * width
    left = []
    cmm_next = cmm_panel[:, :width]
    for chunk in range(N_CHUNKS):
        cmm_c = lax.all_gather(cmm_next, "narrow", axis=1, tiled=True)
        z_c = jnp.dot(r_matrix, cmm_c, preferred_element_type=jnp.float32)
        if chunk + 1 < N_CHUNKS:
            cmm_next, z_c = lax.optimization_barrier(
                (cmm_panel[:, (chunk + 1) * width:(chunk + 2) * width], z_c)
            )
        else:
            rc_all, z_c = lax.optimization_barrier((rc_all, z_c))
        recv = lax.all_to_all(
            z_c.reshape(n_wide, piece, zw), "wide", 0, 0, tiled=True
        )
        z_sum = jnp.sum(recv, axis=0).reshape(piece, n_narrow, width // panel_width, panel_width)
        a_c = (z_sum - ctm_rows[:, :, chunk]).astype(jnp.bfloat16).reshape(piece, zw)
        if chunk == 0:
            a_c = jnp.concatenate([a_c, r_rows], axis=1)
        a_c = lax.ppermute(a_c, ("wide", "narrow"), perm)
        left.append(lax.all_gather(a_c, "narrow", axis=0, tiled=True))

    rc5 = rc_all.reshape(n_narrow, N_CHUNKS, width // panel_width, slope_rows, 2 * panel_width)
    update = None
    for chunk in range(N_CHUNKS):
        a_rows = left[chunk][:, :n_narrow * width].reshape(
            tile_rows, n_narrow, width // panel_width, panel_width
        )
        term = lax.dot_general(
            a_rows, rc5[:, chunk, :, :, :panel_width], (((1, 2, 3), (0, 1, 3)), ((), ())),
            preferred_element_type=jnp.float32,
        )
        update = term if update is None else update + term
    r_rows = left[0][:, n_narrow * width:].reshape(tile_rows, n_wide, panel_width)
    update = update - lax.dot_general(
        r_rows, rc_all[:, :, panel_width:], (((1, 2), (0, 2)), ((), ())),
        preferred_element_type=jnp.float32,
    )
    return cee_in + update


def solution(mesh):
    n_wide, n_narrow = mesh.shape["wide"], mesh.shape["narrow"]
    placed = (P("narrow", "wide"), P("wide", "narrow"), P("narrow", "wide"), P("wide", "narrow"))

    def body(r_matrix, cmm_panel, ctm_panel, cee_in):
        return per_device(r_matrix, cmm_panel, ctm_panel, cee_in, n_wide, n_narrow)

    return jax.shard_map(
        body, mesh=mesh, in_specs=placed, out_specs=P("wide", "narrow"), check_vma=False
    )
```

```python
import jax
import jax.numpy as jnp
from jax import lax
from jax.sharding import PartitionSpec as P


def per_device(r_matrix, cmm_panel, ctm_panel, cee_in, n_wide, n_narrow):
    slope_rows = r_matrix.shape[0]
    tile_rows = cee_in.shape[0]
    panel_width = ctm_panel.shape[1]
    piece = slope_rows // n_wide
    wide_index = lax.axis_index("wide")
    narrow_index = lax.axis_index("narrow")

    rc = jnp.concatenate([r_matrix[:, :panel_width], ctm_panel], axis=1)

    cmm_full = lax.all_gather(cmm_panel, "narrow", axis=1, tiled=True)
    z_part = jnp.dot(r_matrix, cmm_full, preferred_element_type=jnp.float32)
    z_part = jnp.concatenate([z_part, rc.astype(jnp.float32)], axis=1)

    z_recv = lax.all_to_all(
        z_part.reshape(n_wide, piece, z_part.shape[1]), "wide", 0, 0, tiled=True
    )
    n_cols = n_wide * panel_width
    z_mine = jnp.sum(z_recv[:, :, :n_cols], axis=0).reshape(piece, n_wide, panel_width)
    rc_rows = jnp.transpose(z_recv[:, :, n_cols:], (1, 0, 2))
    a_piece = (z_mine - rc_rows[:, :, panel_width:]).astype(jnp.bfloat16)
    left_piece = jnp.concatenate([a_piece, -rc_rows[:, :, :panel_width].astype(jnp.bfloat16)], axis=2)

    rc, z_recv = lax.optimization_barrier((rc, z_recv))
    rc_all = lax.all_to_all(
        jnp.broadcast_to(rc[None], (n_wide,) + rc.shape), "wide", 0, 0, tiled=True
    )

    blocks = n_wide // n_narrow
    perm = []
    for w in range(n_wide):
        for n in range(n_narrow):
            perm.append((w * n_narrow + n, (n * blocks + w // n_narrow) * n_narrow + w % n_narrow))
    left_piece = lax.ppermute(left_piece, ("wide", "narrow"), perm)
    left_rows = lax.all_gather(left_piece, "narrow", axis=0, tiled=True)

    update = lax.dot_general(
        left_rows, rc_all, (((1, 2), (0, 2)), ((), ())), preferred_element_type=jnp.float32
    )
    return cee_in + update


def solution(mesh):
    n_wide, n_narrow = mesh.shape["wide"], mesh.shape["narrow"]
    placed = (P("narrow", "wide"), P("wide", "narrow"), P("narrow", "wide"), P("wide", "narrow"))

    def body(r_matrix, cmm_panel, ctm_panel, cee_in):
        return per_device(r_matrix, cmm_panel, ctm_panel, cee_in, n_wide, n_narrow)

    return jax.shard_map(
        body, mesh=mesh, in_specs=placed, out_specs=P("wide", "narrow"), check_vma=False
    )
```

```python
import jax
import jax.numpy as jnp
from jax import lax
from jax.sharding import PartitionSpec as P


def per_device(r_matrix, cmm_panel, ctm_panel, cee_in, n_wide, n_narrow):
    slope_rows = r_matrix.shape[0]
    tile_rows = cee_in.shape[0]
    panel_width = ctm_panel.shape[1]
    piece = slope_rows // n_wide
    wide_index = lax.axis_index("wide")
    narrow_index = lax.axis_index("narrow")

    rc = jnp.concatenate([r_matrix[:, :panel_width], ctm_panel], axis=1)
    rc_all = lax.all_to_all(
        jnp.broadcast_to(rc[None], (n_wide,) + rc.shape), "wide", 0, 0, tiled=True
    )

    cmm_full = lax.all_gather(cmm_panel, "narrow", axis=1, tiled=True)
    z_part = jnp.dot(r_matrix, cmm_full, preferred_element_type=jnp.float32)

    z_recv = lax.all_to_all(
        z_part.reshape(n_wide, piece, z_part.shape[1]), "wide", 0, 0, tiled=True
    )
    z_mine = jnp.sum(z_recv, axis=0).reshape(piece, n_wide, panel_width)
    rc_rows = lax.dynamic_slice_in_dim(rc_all, wide_index * piece, piece, 1)
    rc_rows = jnp.transpose(rc_rows, (1, 0, 2))
    a_piece = (z_mine - rc_rows[:, :, panel_width:].astype(jnp.float32)).astype(jnp.bfloat16)
    left_piece = jnp.concatenate([a_piece, -rc_rows[:, :, :panel_width]], axis=2)

    blocks = n_wide // n_narrow
    perm = []
    for w in range(n_wide):
        for n in range(n_narrow):
            perm.append((w * n_narrow + n, (n * blocks + w // n_narrow) * n_narrow + w % n_narrow))
    left_piece = lax.ppermute(left_piece, ("wide", "narrow"), perm)
    left_rows = lax.all_to_all(
        jnp.broadcast_to(left_piece[None], (n_narrow,) + left_piece.shape), "narrow", 0, 0, tiled=True
    ).reshape((tile_rows,) + left_piece.shape[1:])

    update = lax.dot_general(
        left_rows, rc_all, (((1, 2), (0, 2)), ((), ())), preferred_element_type=jnp.float32
    )
    return cee_in + update


def solution(mesh):
    n_wide, n_narrow = mesh.shape["wide"], mesh.shape["narrow"]
    placed = (P("narrow", "wide"), P("wide", "narrow"), P("narrow", "wide"), P("wide", "narrow"))

    def body(r_matrix, cmm_panel, ctm_panel, cee_in):
        return per_device(r_matrix, cmm_panel, ctm_panel, cee_in, n_wide, n_narrow)

    return jax.shard_map(
        body, mesh=mesh, in_specs=placed, out_specs=P("wide", "narrow"), check_vma=False
    )
```

```python
import jax
import jax.numpy as jnp
from jax import lax
from jax.sharding import PartitionSpec as P


def _position(w, n, n_wide, n_narrow):
    if (n_wide, n_narrow) == (32, 8):
        x, rest = divmod(w, 8)
        y, z_lo = divmod(rest, 2)
        z_hi, core = divmod(n, 2)
        return (x, y, 2 * z_hi + z_lo), (4, 4, 8)
    return (w, n), (n_wide, n_narrow)


def _hops(a, b, n_wide, n_narrow):
    (pa, sizes), (pb, _) = _position(*a, n_wide, n_narrow), _position(*b, n_wide, n_narrow)
    return sum(min(abs(u - v), size - abs(u - v)) for u, v, size in zip(pa, pb, sizes))


def _routes(n_wide, n_narrow):
    blocks = n_wide // n_narrow
    pieces, perm = [], []
    for n0 in range(n_narrow):
        pairs = sorted(
            (_hops((w, n0), (n0 * blocks + k, m), n_wide, n_narrow), w, k, m)
            for w in range(n_wide) for k in range(blocks) for m in range(n_narrow)
        )
        taken_w, taken_t, row = set(), set(), [0] * n_wide
        for _, w, k, m in pairs:
            if w in taken_w or (k, m) in taken_t:
                continue
            taken_w.add(w)
            taken_t.add((k, m))
            row[w] = k * n_narrow + m
            perm.append((w * n_narrow + n0, (n0 * blocks + k) * n_narrow + m))
        pieces.append(row)
    return pieces, perm


def per_device(r_matrix, cmm_panel, ctm_panel, cee_in, n_wide, n_narrow):
    slope_rows = r_matrix.shape[0]
    tile_rows = cee_in.shape[0]
    panel_width = ctm_panel.shape[1]
    piece = slope_rows // n_wide
    wide_index = lax.axis_index("wide")
    narrow_index = lax.axis_index("narrow")

    rc = jnp.concatenate([r_matrix[:, :panel_width], ctm_panel], axis=1)
    rc_all = lax.all_to_all(
        jnp.broadcast_to(rc[None], (n_wide,) + rc.shape), "wide", 0, 0, tiled=True
    )

    pieces, perm = _routes(n_wide, n_narrow)
    pieces = jnp.asarray(pieces, jnp.int32)
    mine = pieces[narrow_index, wide_index]
    r_sent = jnp.take(
        r_matrix.reshape(n_wide, piece, r_matrix.shape[1]), pieces[narrow_index], axis=0
    ).reshape(r_matrix.shape)

    cmm_full = lax.all_gather(cmm_panel, "narrow", axis=1, tiled=True)
    z_part = jnp.dot(r_sent, cmm_full, preferred_element_type=jnp.float32)

    z_recv = lax.all_to_all(
        z_part.reshape(n_wide, piece, z_part.shape[1]), "wide", 0, 0, tiled=True
    )
    z_mine = jnp.sum(z_recv, axis=0).reshape(piece, n_wide, panel_width)
    rc_rows = lax.dynamic_slice_in_dim(rc_all, mine * piece, piece, 1)
    rc_rows = jnp.transpose(rc_rows, (1, 0, 2))
    a_piece = (z_mine - rc_rows[:, :, panel_width:].astype(jnp.float32)).astype(jnp.bfloat16)
    left_piece = jnp.concatenate([a_piece, -rc_rows[:, :, :panel_width]], axis=2)

    left_piece = lax.ppermute(left_piece, ("wide", "narrow"), perm)
    left_rows = lax.all_gather(left_piece, "narrow", axis=0, tiled=True)

    update = lax.dot_general(
        left_rows, rc_all, (((1, 2), (0, 2)), ((), ())), preferred_element_type=jnp.float32
    )
    return cee_in + update


def solution(mesh):
    n_wide, n_narrow = mesh.shape["wide"], mesh.shape["narrow"]
    placed = (P("narrow", "wide"), P("wide", "narrow"), P("narrow", "wide"), P("wide", "narrow"))

    def body(r_matrix, cmm_panel, ctm_panel, cee_in):
        return per_device(r_matrix, cmm_panel, ctm_panel, cee_in, n_wide, n_narrow)

    return jax.shard_map(
        body, mesh=mesh, in_specs=placed, out_specs=P("wide", "narrow"), check_vma=False
    )
```

```python
import jax
import jax.numpy as jnp
from jax import lax
from jax.sharding import PartitionSpec as P


def _position(w, n, n_wide, n_narrow):
    if (n_wide, n_narrow) == (32, 8):
        x, rest = divmod(w, 8)
        y, z_lo = divmod(rest, 2)
        z_hi, core = divmod(n, 2)
        return (x, y, 2 * z_hi + z_lo), (4, 4, 8)
    return (w, n), (n_wide, n_narrow)


def _hops(a, b, n_wide, n_narrow):
    (pa, sizes), (pb, _) = _position(*a, n_wide, n_narrow), _position(*b, n_wide, n_narrow)
    return sum(min(abs(u - v), size - abs(u - v)) for u, v, size in zip(pa, pb, sizes))


def _routes(n_wide, n_narrow):
    blocks = n_wide // n_narrow
    pieces, perm = [], []
    for n0 in range(n_narrow):
        pairs = sorted(
            (_hops((w, n0), (n0 * blocks + k, m), n_wide, n_narrow), w, k, m)
            for w in range(n_wide) for k in range(blocks) for m in range(n_narrow)
        )
        taken_w, taken_t, row = set(), set(), [0] * n_wide
        for _, w, k, m in pairs:
            if w in taken_w or (k, m) in taken_t:
                continue
            taken_w.add(w)
            taken_t.add((k, m))
            row[w] = k * n_narrow + m
            perm.append((w * n_narrow + n0, (n0 * blocks + k) * n_narrow + m))
        pieces.append(row)
    return pieces, perm


def per_device(r_matrix, cmm_panel, ctm_panel, cee_in, n_wide, n_narrow):
    slope_rows = r_matrix.shape[0]
    tile_rows = cee_in.shape[0]
    panel_width = ctm_panel.shape[1]
    piece = slope_rows // n_wide
    wide_index = lax.axis_index("wide")
    narrow_index = lax.axis_index("narrow")

    rc = jnp.concatenate([r_matrix[:, :panel_width], ctm_panel], axis=1)
    rc_all = lax.all_to_all(
        jnp.broadcast_to(rc[None], (n_wide,) + rc.shape), "wide", 0, 0, tiled=True
    )

    pieces, perm = _routes(n_wide, n_narrow)
    pieces = jnp.asarray(pieces, jnp.int32)
    mine = pieces[narrow_index, wide_index]
    r_sent = jnp.take(
        r_matrix.reshape(n_wide, piece, r_matrix.shape[1]), pieces[narrow_index], axis=0
    ).reshape(r_matrix.shape)

    cmm_full = lax.all_gather(cmm_panel, "narrow", axis=1, tiled=True)
    z_part = jnp.dot(r_sent, cmm_full, preferred_element_type=jnp.float32)

    z_recv = lax.all_to_all(
        z_part.reshape(n_wide, piece, z_part.shape[1]), "wide", 0, 0, tiled=True
    )
    z_mine = jnp.sum(z_recv, axis=0).reshape(piece, n_wide, panel_width)
    rc_rows = lax.dynamic_slice_in_dim(rc_all, mine * piece, piece, 1)
    rc_rows = jnp.transpose(rc_rows, (1, 0, 2))
    a_piece = (z_mine - rc_rows[:, :, panel_width:].astype(jnp.float32)).astype(jnp.bfloat16)
    left_piece = jnp.concatenate([a_piece, -rc_rows[:, :, :panel_width]], axis=2)

    left_piece = lax.ppermute(left_piece, ("wide", "narrow"), perm)
    left_rows = lax.all_gather(left_piece, "narrow", axis=0, tiled=True)

    right = lax.optimization_barrier(
        jnp.transpose(rc_all, (1, 0, 2)).reshape(slope_rows, n_wide * 2 * panel_width)
    )
    update = lax.dot_general(
        left_rows.reshape(tile_rows, -1), right, (((1,), (1,)), ((), ())),
        preferred_element_type=jnp.float32,
    )
    return cee_in + update


def solution(mesh):
    n_wide, n_narrow = mesh.shape["wide"], mesh.shape["narrow"]
    placed = (P("narrow", "wide"), P("wide", "narrow"), P("narrow", "wide"), P("wide", "narrow"))

    def body(r_matrix, cmm_panel, ctm_panel, cee_in):
        return per_device(r_matrix, cmm_panel, ctm_panel, cee_in, n_wide, n_narrow)

    return jax.shard_map(
        body, mesh=mesh, in_specs=placed, out_specs=P("wide", "narrow"), check_vma=False
    )
```

```python
import jax
import jax.numpy as jnp
from jax import lax
from jax.sharding import PartitionSpec as P


def _position(w, n, n_wide, n_narrow):
    if (n_wide, n_narrow) == (32, 8):
        x, rest = divmod(w, 8)
        y, z_lo = divmod(rest, 2)
        z_hi, core = divmod(n, 2)
        return (x, y, 2 * z_hi + z_lo), (4, 4, 8)
    return (w, n), (n_wide, n_narrow)


def _hops(a, b, n_wide, n_narrow):
    (pa, sizes), (pb, _) = _position(*a, n_wide, n_narrow), _position(*b, n_wide, n_narrow)
    return sum(min(abs(u - v), size - abs(u - v)) for u, v, size in zip(pa, pb, sizes))


def _routes(n_wide, n_narrow):
    blocks = n_wide // n_narrow
    pieces, perm = [], []
    for n0 in range(n_narrow):
        pairs = sorted(
            (_hops((w, n0), (n0 * blocks + k, m), n_wide, n_narrow), w, k, m)
            for w in range(n_wide) for k in range(blocks) for m in range(n_narrow)
        )
        taken_w, taken_t, row = set(), set(), [0] * n_wide
        for _, w, k, m in pairs:
            if w in taken_w or (k, m) in taken_t:
                continue
            taken_w.add(w)
            taken_t.add((k, m))
            row[w] = k * n_narrow + m
            perm.append((w * n_narrow + n0, (n0 * blocks + k) * n_narrow + m))
        pieces.append(row)
    return pieces, perm


def per_device(r_matrix, cmm_panel, ctm_panel, cee_in, n_wide, n_narrow):
    slope_rows = r_matrix.shape[0]
    tile_rows = cee_in.shape[0]
    panel_width = ctm_panel.shape[1]
    piece = slope_rows // n_wide
    wide_index = lax.axis_index("wide")
    narrow_index = lax.axis_index("narrow")

    rc = jnp.concatenate([r_matrix[:, :panel_width], ctm_panel], axis=1)
    rc_all = lax.all_to_all(
        jnp.broadcast_to(rc[None], (n_wide,) + rc.shape), "wide", 0, 0, tiled=True
    )

    pieces, perm = _routes(n_wide, n_narrow)
    pieces = jnp.asarray(pieces, jnp.int32)
    mine = pieces[narrow_index, wide_index]
    r_sent = jnp.take(
        r_matrix.reshape(n_wide, piece, r_matrix.shape[1]), pieces[narrow_index], axis=0
    ).reshape(r_matrix.shape)

    cmm_full = lax.all_gather(cmm_panel, "narrow", axis=1, tiled=True)
    z_part = jnp.dot(r_sent, cmm_full, preferred_element_type=jnp.float32)

    z_recv = lax.all_to_all(
        z_part.reshape(n_wide, piece, z_part.shape[1]), "wide", 0, 0, tiled=True
    )
    z_mine = jnp.sum(z_recv, axis=0).reshape(piece, n_wide, panel_width)
    rc_rows = lax.dynamic_slice_in_dim(rc_all, mine * piece, piece, 1)
    rc_rows = jnp.transpose(rc_rows, (1, 0, 2))
    a_piece = (z_mine - rc_rows[:, :, panel_width:].astype(jnp.float32)).astype(jnp.bfloat16)
    left_piece = jnp.concatenate([a_piece, -rc_rows[:, :, :panel_width]], axis=2)

    shape = left_piece.shape
    left_piece = lax.ppermute(left_piece.reshape(piece, -1), ("wide", "narrow"), perm)
    left_rows = lax.all_gather(left_piece, "narrow", axis=0, tiled=True).reshape((tile_rows,) + shape[1:])

    update = lax.dot_general(
        left_rows, rc_all, (((1, 2), (0, 2)), ((), ())), preferred_element_type=jnp.float32
    )
    return cee_in + update


def solution(mesh):
    n_wide, n_narrow = mesh.shape["wide"], mesh.shape["narrow"]
    placed = (P("narrow", "wide"), P("wide", "narrow"), P("narrow", "wide"), P("wide", "narrow"))

    def body(r_matrix, cmm_panel, ctm_panel, cee_in):
        return per_device(r_matrix, cmm_panel, ctm_panel, cee_in, n_wide, n_narrow)

    return jax.shard_map(
        body, mesh=mesh, in_specs=placed, out_specs=P("wide", "narrow"), check_vma=False
    )
```

```python
import jax
import jax.numpy as jnp
from jax import lax
from jax.sharding import PartitionSpec as P


def _position(w, n, n_wide, n_narrow):
    if (n_wide, n_narrow) == (32, 8):
        x, rest = divmod(w, 8)
        y, z_lo = divmod(rest, 2)
        z_hi, core = divmod(n, 2)
        return (x, y, 2 * z_hi + z_lo), (4, 4, 8)
    return (w, n), (n_wide, n_narrow)


def _hops(a, b, n_wide, n_narrow):
    (pa, sizes), (pb, _) = _position(*a, n_wide, n_narrow), _position(*b, n_wide, n_narrow)
    return sum(min(abs(u - v), size - abs(u - v)) for u, v, size in zip(pa, pb, sizes))


def _routes(n_wide, n_narrow):
    blocks = n_wide // n_narrow
    pieces, perm = [], []
    for n0 in range(n_narrow):
        pairs = sorted(
            (_hops((w, n0), (n0 * blocks + k, m), n_wide, n_narrow), w, k, m)
            for w in range(n_wide) for k in range(blocks) for m in range(n_narrow)
        )
        taken_w, taken_t, row = set(), set(), [0] * n_wide
        for _, w, k, m in pairs:
            if w in taken_w or (k, m) in taken_t:
                continue
            taken_w.add(w)
            taken_t.add((k, m))
            row[w] = k * n_narrow + m
            perm.append((w * n_narrow + n0, (n0 * blocks + k) * n_narrow + m))
        pieces.append(row)
    return pieces, perm


def per_device(r_matrix, cmm_panel, ctm_panel, cee_in, n_wide, n_narrow):
    slope_rows = r_matrix.shape[0]
    tile_rows = cee_in.shape[0]
    panel_width = ctm_panel.shape[1]
    piece = slope_rows // n_wide
    wide_index = lax.axis_index("wide")
    narrow_index = lax.axis_index("narrow")

    rc = jnp.concatenate([r_matrix[:, :panel_width], ctm_panel], axis=1)
    rc_all = lax.all_to_all(
        jnp.broadcast_to(rc[None], (n_wide,) + rc.shape), "wide", 0, 0, tiled=True
    )

    pieces, perm = _routes(n_wide, n_narrow)
    pieces = jnp.asarray(pieces, jnp.int32)
    mine = pieces[narrow_index, wide_index]
    r_sent = jnp.take(
        r_matrix.reshape(n_wide, piece, r_matrix.shape[1]), pieces[narrow_index], axis=0
    ).reshape(r_matrix.shape)

    cmm_full = lax.all_gather(cmm_panel, "narrow", axis=1, tiled=True)
    z_part = jnp.dot(r_sent, cmm_full, preferred_element_type=jnp.float32)

    z_recv = lax.all_to_all(
        z_part.reshape(n_wide, piece, z_part.shape[1]), "wide", 0, 0, tiled=True
    )
    z_mine = jnp.sum(z_recv, axis=0).reshape(piece, n_wide, panel_width)
    rc_rows = lax.dynamic_slice_in_dim(rc_all, mine * piece, piece, 1)
    rc_rows = jnp.transpose(rc_rows, (1, 0, 2))
    a_piece = (z_mine - rc_rows[:, :, panel_width:].astype(jnp.float32)).astype(jnp.bfloat16)
    left_piece = jnp.concatenate([a_piece, -rc_rows[:, :, :panel_width]], axis=2)

    shape = left_piece.shape
    left_piece = lax.ppermute(left_piece.reshape(piece, -1), ("wide", "narrow"), perm)
    left_rows = lax.all_gather(left_piece, "narrow", axis=0, tiled=True)

    right = jnp.transpose(rc_all, (1, 0, 2)).reshape(slope_rows, -1)
    update = lax.dot_general(
        right, left_rows, (((1,), (1,)), ((), ())), preferred_element_type=jnp.float32
    ).T
    return cee_in + update


def solution(mesh):
    n_wide, n_narrow = mesh.shape["wide"], mesh.shape["narrow"]
    placed = (P("narrow", "wide"), P("wide", "narrow"), P("narrow", "wide"), P("wide", "narrow"))

    def body(r_matrix, cmm_panel, ctm_panel, cee_in):
        return per_device(r_matrix, cmm_panel, ctm_panel, cee_in, n_wide, n_narrow)

    return jax.shard_map(
        body, mesh=mesh, in_specs=placed, out_specs=P("wide", "narrow"), check_vma=False
    )
```
